128 devices in a mesh: blk: 4 (over x_hi, core), aux: 32 (over x_lo, y, z).
Axes of the slice: x: 4 (x_hi: 2, x_lo: 2; x = x_hi * 2 + x_lo), y: 4, z: 4, core: 2. Of those that a mesh axis runs over, the one named last changes fastest.
Arguments:
- tensor: bfloat16 [512, 512, 4096], P('blk', None, 'aux'), may hold values from -0.25 to 0.25
- greens: bfloat16 [2, 512, 512], P(None, None, 'blk'), may hold values from -0.25 to 0.25
- pattern: int32 [4, 4, 32], P('blk', None, 'aux'), may hold values from 0 to 1, as said below
- block_sizes: int32 [4], replicated, may hold values from 64 to 128, as said below
- trial_vectors: bfloat16 [4096, 32], P('aux'), may hold values from -0.09375 to 0.09375
Outputs:
- response: float32 [32, 4096], P('blk', 'aux')
The draws below stay inside these ranges and needn't reach their ends.
Inputs may be any that keep to these rules, and one draw needn't show every extreme that they name: pattern[mu, nu, p] is 1 exactly where |mu - nu| is at most a reach drawn for auxiliary block p, so every diagonal entry is 1. The first block_sizes[b] basis functions of atom block b are live, the rest are padding; some block is full and some block has exactly half of its functions live.
All inputs are finite; a program needn't handle non-finite values.
Results may differ from the reference program's by a relative error of at most 0.0049.
Values may be sent and summed in bfloat16 or wider, within the bound.
No kernel may reach another device: no remote copies, remote signals or barrier semaphores. Data moves between devices by JAX's collectives and lax.ppermute only.
A program may use at most 256 MiB of HBM per device.

```python
import jax
import jax.numpy as jnp
from jax import lax

BS = 128
PS = 128
NV = 32
NB = 4
NPB = 32
NBAS = 512
NAUX = 4096


def draw_pattern(key, part):
    reach_steps = jax.random.randint(key, (NPB,), 0, NB)
    distance = jnp.abs(jnp.arange(NB)[:, None] - jnp.arange(NB)[None, :])
    return (distance[:, :, None] <= reach_steps[None, None, :]).astype(jnp.int32)


def draw_block_sizes(key, part):
    counts = jax.random.randint(key, (NB,), BS // 2, BS + 1)
    chosen = jax.random.randint(jax.random.fold_in(key, 7), (), 0, NB)
    halved = (chosen + 1) % NB
    positions = jnp.arange(NB)
    counts = jnp.where(positions == halved, BS // 2, counts)
    return jnp.where(positions == chosen, BS, counts).astype(jnp.int32)


def level_of(own_key, extent, pieces, least, high):
    def one(axis_at, shards_of):
        draws = jax.random.uniform(jax.random.fold_in(jax.random.fold_in(own_key, 6), axis_at), (shards_of,), jnp.float32, least / len(pieces), high / len(pieces))
        return jnp.repeat(jnp.exp(draws), extent[axis_at] // shards_of).reshape((-1,) + (1,) * (len(extent) - axis_at - 1))

    gain = one(*pieces[0])
    for cut in pieces[1:]:
        gain = gain * one(*cut)
    return gain


def noise(stream_key, dims, width, most, pieces=(), kind=jnp.bfloat16):
    factor_of = level_of(stream_key, dims, pieces, -0.22, 0.18) if pieces else 1.0
    drawn = jax.random.normal(stream_key, dims, jnp.float32) * width * factor_of
    return jnp.minimum(jnp.maximum(drawn, -most), most).astype(kind)


def setup_inputs(seed: int = 0) -> dict:
    key_of = jax.random.split(jax.random.key(seed), 6)
    return {
        "tensor": noise(key_of[0], (NBAS, NBAS, NAUX), NBAS ** -0.5, 0.25, ((0, 4), (2, 32))),
        "greens": noise(key_of[1], (2, NBAS, NBAS), NBAS ** -0.5, 0.25, ((2, 4),)),
        "pattern": draw_pattern(jax.random.fold_in(key_of[5], 71), 0),
        "block_sizes": draw_block_sizes(jax.random.fold_in(key_of[5], 71), 0),
        "trial_vectors": noise(key_of[4], (NAUX, NV), NAUX ** -0.5, 0.09375, ((0, 32),)),
    }


def reference(tensor, greens, pattern, block_sizes, trial_vectors):
    live_mask = (jnp.arange(BS)[None, :] < block_sizes[:, None]).reshape(NBAS)
    occupied = greens[0].astype(jnp.float32)
    virtual = greens[1].astype(jnp.float32)

    def screen(block_index):
        aux_block = lax.dynamic_slice_in_dim(tensor, block_index * PS, PS, 2)
        tile_mask = lax.dynamic_index_in_dim(pattern, block_index, 2, False)
        keep_mask = jnp.broadcast_to(tile_mask[:, None, :, None] > 0, (NB, BS, NB, BS)).reshape(NBAS, NBAS)
        keep_mask = keep_mask & live_mask[:, None] & live_mask[None, :]
        return jnp.where(keep_mask[:, :, None], aux_block, jnp.zeros_like(aux_block)).astype(jnp.float32)

    def project(running, block_index):
        screened = screen(block_index)
        right_half = jnp.einsum("lsq,sn->lnq", screened, virtual).astype(jnp.bfloat16)
        right_half = lax.optimization_barrier(right_half).astype(jnp.float32)
        vectors = lax.dynamic_slice_in_dim(trial_vectors, block_index * PS, PS, 0).astype(jnp.float32)
        return running + jnp.einsum("lnq,qk->lnk", right_half, vectors), None

    block_ids = jnp.arange(NPB, dtype=jnp.int32)
    projected, _ = lax.scan(project, jnp.zeros((NBAS, NBAS, NV), jnp.float32), block_ids)
    projected = lax.optimization_barrier(projected.astype(jnp.bfloat16)).astype(jnp.float32)

    def respond(block_index):
        screened = screen(block_index)
        left_half = jnp.einsum("nsp,sl->nlp", screened, occupied).astype(jnp.bfloat16)
        left_half = lax.optimization_barrier(left_half).astype(jnp.float32)
        return jnp.einsum("nlp,lnk->kp", left_half, projected)

    blocks = lax.map(respond, block_ids)
    return jnp.transpose(blocks, (1, 0, 2)).reshape(NV, NAUX)
```

```python
import jax
import jax.numpy as jnp
from jax import lax
from jax.sharding import PartitionSpec as P

BS = 128
PS = 128
MB_DEV = 1
PB_DEV = 1
HI = lax.Precision.HIGHEST


def per_device(tensor, greens, pattern, block_sizes, trial_vectors):
    shard_rows = tensor.shape[0]
    basis_count = tensor.shape[1]
    aux_local = tensor.shape[2]
    block_count = block_sizes.shape[0]
    live_mask = (jnp.arange(BS)[None, :] < block_sizes[:, None]).reshape(basis_count)
    row_live = lax.dynamic_slice_in_dim(live_mask, lax.axis_index("blk") * shard_rows, shard_rows)
    tile_mask = jnp.broadcast_to(
        pattern[:, None, :, None, :, None] > 0, (MB_DEV, BS, block_count, BS, PB_DEV, PS)
    )
    keep_mask = tile_mask.reshape(shard_rows, basis_count, aux_local)
    keep_mask = keep_mask & row_live[:, None, None] & live_mask[None, :, None]
    screened = jnp.where(keep_mask, tensor, jnp.zeros_like(tensor))

    weighted = jnp.einsum(
        "rsp,pk->krs", screened, trial_vectors, preferred_element_type=jnp.float32
    )
    weighted = lax.psum_scatter(weighted, "aux", scatter_dimension=0, tiled=True)[0]
    virtual = lax.all_gather(greens[1], "blk", axis=1, tiled=True).astype(jnp.float32)
    occupied_cols = greens[0].astype(jnp.float32)
    projected = jnp.dot(weighted, virtual, precision=HI)
    z_part = jnp.einsum("ln,sl->ns", projected, occupied_cols, precision=HI)
    z_rows = lax.psum_scatter(z_part, "blk", scatter_dimension=0, tiled=True)
    z_all = lax.all_gather(z_rows.astype(jnp.bfloat16), "aux", axis=0, tiled=False)
    terms = jnp.einsum(
        "nsp,kns->kp", screened, z_all, preferred_element_type=jnp.float32
    )
    return lax.psum_scatter(terms, "blk", scatter_dimension=0, tiled=True)


def solution(mesh):
    placed = (
        P("blk", None, "aux"),
        P(None, None, "blk"),
        P("blk", None, "aux"),
        P(),
        P("aux", None),
    )
    return jax.shard_map(
        per_device, mesh=mesh, in_specs=placed, out_specs=P("blk", "aux"), check_vma=False
    )
```

```python
import jax
import jax.numpy as jnp
from jax import lax
from jax.sharding import PartitionSpec as P

BS = 128
PS = 128
MB_DEV = 1
PB_DEV = 1
HI = lax.Precision.HIGHEST


def per_device(tensor, greens, pattern, block_sizes, trial_vectors):
    shard_rows = tensor.shape[0]
    basis_count = tensor.shape[1]
    aux_local = tensor.shape[2]
    block_count = block_sizes.shape[0]
    live_mask = (jnp.arange(BS)[None, :] < block_sizes[:, None]).reshape(basis_count)
    row_live = lax.dynamic_slice_in_dim(live_mask, lax.axis_index("blk") * shard_rows, shard_rows)
    tile_mask = jnp.broadcast_to(
        pattern[:, None, :, None, :, None] > 0, (MB_DEV, BS, block_count, BS, PB_DEV, PS)
    )
    keep_mask = tile_mask.reshape(shard_rows, basis_count, aux_local)
    keep_mask = keep_mask & row_live[:, None, None] & live_mask[None, :, None]
    screened = jnp.where(keep_mask, tensor, jnp.zeros_like(tensor))

    weighted = jnp.einsum(
        "rsp,pk->krs", screened, trial_vectors, preferred_element_type=jnp.float32
    )
    weighted = lax.all_to_all(weighted, "aux", split_axis=0, concat_axis=0, tiled=True)
    weighted = jnp.sum(weighted, axis=0)
    virtual = lax.all_gather(greens[1], "blk", axis=1, tiled=True).astype(jnp.float32)
    occupied_cols = greens[0].astype(jnp.float32)
    projected = jnp.dot(weighted, virtual, precision=HI)
    z_part = jnp.einsum("ln,sl->ns", projected, occupied_cols, precision=HI)
    z_rows = lax.psum_scatter(z_part, "blk", scatter_dimension=0, tiled=True)
    aux_count = lax.axis_size("aux")
    z_copies = jnp.broadcast_to(z_rows.astype(jnp.bfloat16)[None], (aux_count,) + z_rows.shape)
    z_all = lax.all_to_all(z_copies, "aux", split_axis=0, concat_axis=0, tiled=True)
    terms = jnp.einsum(
        "nsp,kns->kp", screened, z_all, preferred_element_type=jnp.float32
    )
    return lax.psum_scatter(terms, "blk", scatter_dimension=0, tiled=True)


def solution(mesh):
    placed = (
        P("blk", None, "aux"),
        P(None, None, "blk"),
        P("blk", None, "aux"),
        P(),
        P("aux", None),
    )
    return jax.shard_map(
        per_device, mesh=mesh, in_specs=placed, out_specs=P("blk", "aux"), check_vma=False
    )
```

```python
import jax
import jax.numpy as jnp
from jax import lax
from jax.sharding import PartitionSpec as P

BS = 128
PS = 128
MB_DEV = 1
PB_DEV = 1
HI = lax.Precision.HIGHEST


def per_device(tensor, greens, pattern, block_sizes, trial_vectors):
    shard_rows = tensor.shape[0]
    basis_count = tensor.shape[1]
    aux_local = tensor.shape[2]
    block_count = block_sizes.shape[0]
    live_mask = (jnp.arange(BS)[None, :] < block_sizes[:, None]).reshape(basis_count)
    row_live = lax.dynamic_slice_in_dim(live_mask, lax.axis_index("blk") * shard_rows, shard_rows)
    tile_mask = jnp.broadcast_to(
        pattern[:, None, :, None, :, None] > 0, (MB_DEV, BS, block_count, BS, PB_DEV, PS)
    )
    keep_mask = tile_mask.reshape(shard_rows, basis_count, aux_local)
    keep_mask = keep_mask & row_live[:, None, None] & live_mask[None, :, None]
    screened = jnp.where(keep_mask, tensor, jnp.zeros_like(tensor))

    weighted = jnp.einsum(
        "rsp,pk->krs", screened, trial_vectors, preferred_element_type=jnp.float32
    )
    weighted = lax.all_to_all(
        weighted.astype(jnp.bfloat16), "aux", split_axis=0, concat_axis=0, tiled=True
    )
    weighted = jnp.sum(weighted.astype(jnp.float32), axis=0)
    virtual = lax.all_gather(greens[1], "blk", axis=1, tiled=True).astype(jnp.float32)
    occupied_cols = greens[0].astype(jnp.float32)
    projected = jnp.dot(weighted, virtual, precision=HI)
    z_part = jnp.einsum("ln,sl->ns", projected, occupied_cols, precision=HI)
    group_count = lax.axis_size("blk")
    z_part = z_part.reshape((group_count, -1) + z_part.shape[1:])
    z_rows = jnp.sum(lax.all_to_all(z_part, "blk", split_axis=0, concat_axis=0, tiled=True), axis=0)
    aux_count = lax.axis_size("aux")
    z_copies = jnp.broadcast_to(z_rows.astype(jnp.bfloat16)[None], (aux_count,) + z_rows.shape)
    z_all = lax.all_to_all(z_copies, "aux", split_axis=0, concat_axis=0, tiled=True)
    terms = jnp.einsum(
        "nsp,kns->kp", screened, z_all, preferred_element_type=jnp.float32
    )
    terms = terms.reshape((group_count, -1) + terms.shape[1:])
    return jnp.sum(lax.all_to_all(terms, "blk", split_axis=0, concat_axis=0, tiled=True), axis=0)


def solution(mesh):
    placed = (
        P("blk", None, "aux"),
        P(None, None, "blk"),
        P("blk", None, "aux"),
        P(),
        P("aux", None),
    )
    return jax.shard_map(
        per_device, mesh=mesh, in_specs=placed, out_specs=P("blk", "aux"), check_vma=False
    )
```

```python
import jax
import jax.numpy as jnp
from jax import lax
from jax.sharding import PartitionSpec as P

BS = 128
HI = lax.Precision.HIGHEST


def per_device(tensor, greens, pattern, block_sizes, trial_vectors):
    shard_rows = tensor.shape[0]
    basis_count = tensor.shape[1]
    group_count = lax.axis_size("blk")
    aux_count = lax.axis_size("aux")
    block_count = block_sizes.shape[0]
    live_mask = (jnp.arange(BS)[None, :] < block_sizes[:, None]).reshape(basis_count)
    row_live = lax.dynamic_slice_in_dim(live_mask, lax.axis_index("blk") * shard_rows, shard_rows)
    col_keep = jnp.broadcast_to(pattern[0, :, 0][:, None] > 0, (block_count, BS)).reshape(basis_count)
    keep = row_live[:, None] & (col_keep & live_mask)[None, :]

    weighted = jnp.einsum(
        "rsp,pk->krs", tensor, trial_vectors, preferred_element_type=jnp.float32
    )
    weighted = jnp.where(keep[None], weighted, 0.0)
    weighted = lax.all_to_all(
        weighted.astype(jnp.bfloat16), "aux", split_axis=0, concat_axis=0, tiled=True
    )
    weighted = jnp.sum(weighted.astype(jnp.float32), axis=0)
    both = lax.all_gather(greens, "blk", axis=2, tiled=True).astype(jnp.float32)
    occupied = both[0]
    virtual = both[1]
    projected = jnp.dot(weighted, virtual, precision=HI)
    projected = projected.reshape(shard_rows, group_count, shard_rows).transpose(1, 0, 2)
    projected = lax.all_to_all(projected, "blk", split_axis=0, concat_axis=0, tiled=True)
    projected = projected.reshape(group_count * shard_rows, shard_rows)
    z_rows = jnp.einsum("ln,sl->ns", projected, occupied, precision=HI)
    z_copies = jnp.broadcast_to(z_rows.astype(jnp.bfloat16)[None], (aux_count,) + z_rows.shape)
    z_all = lax.all_to_all(z_copies, "aux", split_axis=0, concat_axis=0, tiled=True)
    z_all = jnp.where(keep[None], z_all, jnp.zeros_like(z_all))
    terms = jnp.einsum(
        "nsp,kns->kp", tensor, z_all, preferred_element_type=jnp.float32
    )
    terms = terms.reshape((group_count, -1) + terms.shape[1:])
    return jnp.sum(lax.all_to_all(terms, "blk", split_axis=0, concat_axis=0, tiled=True), axis=0)


def solution(mesh):
    placed = (
        P("blk", None, "aux"),
        P(None, None, "blk"),
        P("blk", None, "aux"),
        P(),
        P("aux", None),
    )
    return jax.shard_map(
        per_device, mesh=mesh, in_specs=placed, out_specs=P("blk", "aux"), check_vma=False
    )
```

```python
import jax
import jax.numpy as jnp
from jax import lax
from jax.sharding import PartitionSpec as P

BS = 128
HI = lax.Precision.HIGHEST
W_CHUNKS = 2


def per_device(tensor, greens, pattern, block_sizes, trial_vectors):
    shard_rows = tensor.shape[0]
    basis_count = tensor.shape[1]
    group_count = lax.axis_size("blk")
    aux_count = lax.axis_size("aux")
    block_count = block_sizes.shape[0]
    live_mask = (jnp.arange(BS)[None, :] < block_sizes[:, None]).reshape(basis_count)
    row_live = lax.dynamic_slice_in_dim(live_mask, lax.axis_index("blk") * shard_rows, shard_rows)
    col_keep = jnp.broadcast_to(pattern[0, :, 0][:, None] > 0, (block_count, BS)).reshape(basis_count)
    keep = row_live[:, None] & (col_keep & live_mask)[None, :]

    chunk_rows = shard_rows // W_CHUNKS
    pieces = []
    for c in range(W_CHUNKS):
        rows = slice(c * chunk_rows, (c + 1) * chunk_rows)
        part = jnp.einsum(
            "rsp,pk->krs", tensor[rows], trial_vectors, preferred_element_type=jnp.float32
        )
        part = jnp.where(keep[None, rows], part, 0.0)
        part = lax.all_to_all(
            part.astype(jnp.bfloat16), "aux", split_axis=0, concat_axis=0, tiled=True
        )
        pieces.append(jnp.sum(part.astype(jnp.float32), axis=0))
    weighted = jnp.concatenate(pieces, axis=0)
    green_copies = jnp.broadcast_to(greens[None], (group_count,) + greens.shape)
    both = lax.all_to_all(green_copies, "blk", split_axis=0, concat_axis=0, tiled=True)
    both = jnp.concatenate(list(both), axis=2).astype(jnp.float32)
    occupied = both[0]
    virtual = both[1]
    projected = jnp.dot(weighted, virtual, precision=HI)
    projected = projected.reshape(shard_rows, group_count, shard_rows).transpose(1, 0, 2)
    projected = lax.all_to_all(projected, "blk", split_axis=0, concat_axis=0, tiled=True)
    projected = projected.reshape(group_count * shard_rows, shard_rows)
    z_rows = jnp.einsum("ln,sl->ns", projected, occupied, precision=HI)
    z_copies = jnp.broadcast_to(z_rows.astype(jnp.bfloat16)[None], (aux_count,) + z_rows.shape)
    z_all = lax.all_to_all(z_copies, "aux", split_axis=0, concat_axis=0, tiled=True)
    z_all = jnp.where(keep[None], z_all, jnp.zeros_like(z_all))
    terms = jnp.einsum(
        "nsp,kns->kp", tensor, z_all, preferred_element_type=jnp.float32
    )
    terms = terms.reshape((group_count, -1) + terms.shape[1:])
    return jnp.sum(lax.all_to_all(terms, "blk", split_axis=0, concat_axis=0, tiled=True), axis=0)


def solution(mesh):
    placed = (
        P("blk", None, "aux"),
        P(None, None, "blk"),
        P("blk", None, "aux"),
        P(),
        P("aux", None),
    )
    return jax.shard_map(
        per_device, mesh=mesh, in_specs=placed, out_specs=P("blk", "aux"), check_vma=False
    )
```

```python
import jax
import jax.numpy as jnp
from jax import lax
from jax.sharding import PartitionSpec as P

BS = 128
HI = lax.Precision.HIGHEST
W_CHUNKS = 2


def per_device(tensor, greens, pattern, block_sizes, trial_vectors):
    shard_rows = tensor.shape[0]
    basis_count = tensor.shape[1]
    group_count = lax.axis_size("blk")
    aux_count = lax.axis_size("aux")
    block_count = block_sizes.shape[0]
    live_mask = (jnp.arange(BS)[None, :] < block_sizes[:, None]).reshape(basis_count)
    row_live = lax.dynamic_slice_in_dim(live_mask, lax.axis_index("blk") * shard_rows, shard_rows)
    col_keep = jnp.broadcast_to(pattern[0, :, 0][:, None] > 0, (block_count, BS)).reshape(basis_count)
    keep = row_live[:, None] & (col_keep & live_mask)[None, :]

    chunk_rows = shard_rows // W_CHUNKS
    pieces = []
    for c in range(W_CHUNKS):
        rows = slice(c * chunk_rows, (c + 1) * chunk_rows)
        part = jnp.einsum(
            "rsp,pk->krs", tensor[rows], trial_vectors, preferred_element_type=jnp.float32
        )
        part = jnp.where(keep[None, rows], part, 0.0)
        part = lax.all_to_all(
            part.astype(jnp.bfloat16), "aux", split_axis=0, concat_axis=0, tiled=True
        )
        pieces.append(jnp.sum(part.astype(jnp.float32), axis=0))
    weighted = jnp.concatenate(pieces, axis=0)
    shifted = [greens] + [
        lax.ppermute(greens, "blk", [(i, (i - s) % group_count) for i in range(group_count)])
        for s in range(1, group_count)
    ]
    both = jnp.roll(jnp.stack(shifted), lax.axis_index("blk"), axis=0)
    both = jnp.concatenate(list(both), axis=2).astype(jnp.float32)
    occupied = both[0]
    virtual = both[1]
    projected = jnp.dot(weighted, virtual, precision=HI)
    projected = projected.reshape(shard_rows, group_count, shard_rows).transpose(1, 0, 2)
    projected = lax.all_to_all(projected, "blk", split_axis=0, concat_axis=0, tiled=True)
    projected = projected.reshape(group_count * shard_rows, shard_rows)
    z_rows = jnp.einsum("ln,sl->ns", projected, occupied, precision=HI)
    z_copies = jnp.broadcast_to(z_rows.astype(jnp.bfloat16)[None], (aux_count,) + z_rows.shape)
    z_all = lax.all_to_all(z_copies, "aux", split_axis=0, concat_axis=0, tiled=True)
    z_all = jnp.where(keep[None], z_all, jnp.zeros_like(z_all))
    terms = jnp.einsum(
        "nsp,kns->kp", tensor, z_all, preferred_element_type=jnp.float32
    )
    terms = terms.reshape((group_count, -1) + terms.shape[1:])
    return jnp.sum(lax.all_to_all(terms, "blk", split_axis=0, concat_axis=0, tiled=True), axis=0)


def solution(mesh):
    placed = (
        P("blk", None, "aux"),
        P(None, None, "blk"),
        P("blk", None, "aux"),
        P(),
        P("aux", None),
    )
    return jax.shard_map(
        per_device, mesh=mesh, in_specs=placed, out_specs=P("blk", "aux"), check_vma=False
    )
```

```python
import jax
import jax.numpy as jnp
from jax import lax
from jax.sharding import PartitionSpec as P

BS = 128
HI = lax.Precision.HIGHEST
W_CHUNKS = 2
AUX_X, AUX_Y, AUX_Z = 2, 4, 4


def per_device(tensor, greens, pattern, block_sizes, trial_vectors):
    shard_rows = tensor.shape[0]
    basis_count = tensor.shape[1]
    group_count = lax.axis_size("blk")
    aux_count = lax.axis_size("aux")
    block_count = block_sizes.shape[0]
    live_mask = (jnp.arange(BS)[None, :] < block_sizes[:, None]).reshape(basis_count)
    row_live = lax.dynamic_slice_in_dim(live_mask, lax.axis_index("blk") * shard_rows, shard_rows)
    col_keep = jnp.broadcast_to(pattern[0, :, 0][:, None] > 0, (block_count, BS)).reshape(basis_count)
    keep = row_live[:, None] & (col_keep & live_mask)[None, :]

    chunk_rows = shard_rows // W_CHUNKS
    pieces = []
    for c in range(W_CHUNKS):
        rows = slice(c * chunk_rows, (c + 1) * chunk_rows)
        part = jnp.einsum(
            "rsp,pk->krs", tensor[rows], trial_vectors, preferred_element_type=jnp.float32
        )
        part = jnp.where(keep[None, rows], part, 0.0)
        part = lax.all_to_all(
            part.astype(jnp.bfloat16), "aux", split_axis=0, concat_axis=0, tiled=True
        )
        pieces.append(jnp.sum(part.astype(jnp.float32), axis=0))
    weighted = jnp.concatenate(pieces, axis=0)
    shifted = [greens] + [
        lax.ppermute(greens, "blk", [(i, (i - s) % group_count) for i in range(group_count)])
        for s in range(1, group_count)
    ]
    both = jnp.roll(jnp.stack(shifted), lax.axis_index("blk"), axis=0)
    both = jnp.concatenate(list(both), axis=2).astype(jnp.float32)
    occupied = both[0]
    virtual = both[1]
    projected = jnp.dot(weighted, virtual, precision=HI)
    projected = projected.reshape(shard_rows, group_count, shard_rows).transpose(1, 0, 2)
    projected = lax.all_to_all(projected, "blk", split_axis=0, concat_axis=0, tiled=True)
    projected = projected.reshape(group_count * shard_rows, shard_rows)
    z_rows = jnp.einsum("ln,sl->ns", projected, occupied, precision=HI)
    z_piece = z_rows.astype(jnp.bfloat16)
    x_recv = lax.ppermute(z_piece, "aux", _shift(0, 1))
    x_both = jnp.stack([z_piece, x_recv])
    half = shard_rows // 2
    first = _ring_gather(_ring_gather(x_both[:, :half], 2), 1)
    second = _ring_gather(_ring_gather(x_both[:, half:], 1), 2)
    first = first.reshape((aux_count, half, basis_count))
    second = second.reshape((aux_count, half, basis_count))
    first = jnp.where(keep[None, :half], first, jnp.zeros_like(first))
    second = jnp.where(keep[None, half:], second, jnp.zeros_like(second))
    terms_first = jnp.einsum(
        "nsp,kns->kp", tensor[:half], first, preferred_element_type=jnp.float32
    )
    terms_second = jnp.einsum(
        "nsp,kns->kp", tensor[half:], second, preferred_element_type=jnp.float32
    )
    me = lax.axis_index("aux")
    mine = (me // (AUX_Y * AUX_Z), (me // AUX_Z) % AUX_Y, me % AUX_Z)
    k = jnp.arange(aux_count)
    theirs = (k // (AUX_Y * AUX_Z), (k // AUX_Z) % AUX_Y, k % AUX_Z)
    dx = (theirs[0] - mine[0]) % AUX_X
    dy = (theirs[1] - mine[1]) % AUX_Y
    dz = (theirs[2] - mine[2]) % AUX_Z
    terms = jnp.take(terms_first, (dy * AUX_Z + dz) * AUX_X + dx, axis=0) + jnp.take(
        terms_second, (dz * AUX_Y + dy) * AUX_X + dx, axis=0
    )
    terms = terms.reshape((group_count, -1) + terms.shape[1:])
    return jnp.sum(lax.all_to_all(terms, "blk", split_axis=0, concat_axis=0, tiled=True), axis=0)


def _shift(axis, step):
    sizes = (AUX_X, AUX_Y, AUX_Z)
    pairs = []
    for i in range(AUX_X * AUX_Y * AUX_Z):
        c = [i // (AUX_Y * AUX_Z), (i // AUX_Z) % AUX_Y, i % AUX_Z]
        c[axis] = (c[axis] + step) % sizes[axis]
        pairs.append((i, (c[0] * AUX_Y + c[1]) * AUX_Z + c[2]))
    return pairs


def _ring_gather(block, axis):
    from_next = lax.ppermute(block, "aux", _shift(axis, -1))
    from_prev = lax.ppermute(block, "aux", _shift(axis, 1))
    cut = block.shape[-2] // 2
    far_a = lax.ppermute(from_next[..., :cut, :], "aux", _shift(axis, -1))
    far_b = lax.ppermute(from_prev[..., cut:, :], "aux", _shift(axis, 1))
    far = jnp.concatenate([far_a, far_b], axis=-2)
    return jnp.stack([block, from_next, far, from_prev])


def solution(mesh):
    placed = (
        P("blk", None, "aux"),
        P(None, None, "blk"),
        P("blk", None, "aux"),
        P(),
        P("aux", None),
    )
    return jax.shard_map(
        per_device, mesh=mesh, in_specs=placed, out_specs=P("blk", "aux"), check_vma=False
    )
```

```python
import jax
import jax.numpy as jnp
from jax import lax
from jax.sharding import PartitionSpec as P

BS = 128
HI = lax.Precision.HIGHEST
W_CHUNKS = 2


def per_device(tensor, greens, pattern, block_sizes, trial_vectors):
    shard_rows = tensor.shape[0]
    basis_count = tensor.shape[1]
    group_count = lax.axis_size("blk")
    aux_count = lax.axis_size("aux")
    block_count = block_sizes.shape[0]
    live_mask = (jnp.arange(BS)[None, :] < block_sizes[:, None]).reshape(basis_count)
    row_live = lax.dynamic_slice_in_dim(live_mask, lax.axis_index("blk") * shard_rows, shard_rows)
    col_keep = jnp.broadcast_to(pattern[0, :, 0][:, None] > 0, (block_count, BS)).reshape(basis_count)
    keep = row_live[:, None] & (col_keep & live_mask)[None, :]

    chunk_rows = shard_rows // W_CHUNKS
    pieces = []
    for c in range(W_CHUNKS):
        rows = slice(c * chunk_rows, (c + 1) * chunk_rows)
        part = jnp.einsum(
            "rsp,pk->krs", tensor[rows], trial_vectors, preferred_element_type=jnp.float32
        )
        part = jnp.where(keep[None, rows], part, 0.0)
        part = lax.all_to_all(
            part.astype(jnp.bfloat16), "aux", split_axis=0, concat_axis=0, tiled=True
        )
        pieces.append(jnp.sum(part.astype(jnp.float32), axis=0))
    weighted = jnp.concatenate(pieces, axis=0)
    shifted = [greens] + [
        lax.ppermute(greens, "blk", [(i, (i - s) % group_count) for i in range(group_count)])
        for s in range(1, group_count)
    ]
    both = jnp.roll(jnp.stack(shifted), lax.axis_index("blk"), axis=0)
    both = jnp.concatenate(list(both), axis=2).astype(jnp.float32)
    occupied = both[0]
    virtual = both[1]
    projected = jnp.dot(weighted, virtual, precision=HI)
    projected = projected.reshape(shard_rows, group_count, shard_rows).transpose(1, 0, 2)
    projected = _blk_exchange(projected, group_count)
    projected = projected.reshape(group_count * shard_rows, shard_rows)
    z_rows = jnp.einsum("ln,sl->ns", projected, occupied, precision=HI)
    z_copies = jnp.broadcast_to(z_rows.astype(jnp.bfloat16)[None], (aux_count,) + z_rows.shape)
    z_all = lax.all_to_all(z_copies, "aux", split_axis=0, concat_axis=0, tiled=True)
    z_all = jnp.where(keep[None], z_all, jnp.zeros_like(z_all))
    terms = jnp.einsum(
        "nsp,kns->kp", tensor, z_all, preferred_element_type=jnp.float32
    )
    terms = terms.reshape((group_count, -1) + terms.shape[1:])
    return jnp.sum(_blk_exchange(terms, group_count), axis=0)


def _blk_exchange(blocks, group_count):
    me = lax.axis_index("blk")
    got = [jnp.take(blocks, me, axis=0)]
    for s in range(1, group_count):
        sent = jnp.take(blocks, (me + s) % group_count, axis=0)
        got.append(
            lax.ppermute(sent, "blk", [(i, (i + s) % group_count) for i in range(group_count)])
        )
    ahead = jnp.stack([got[0]] + got[:0:-1])
    return jnp.roll(ahead, me, axis=0)


def solution(mesh):
    placed = (
        P("blk", None, "aux"),
        P(None, None, "blk"),
        P("blk", None, "aux"),
        P(),
        P("aux", None),
    )
    return jax.shard_map(
        per_device, mesh=mesh, in_specs=placed, out_specs=P("blk", "aux"), check_vma=False
    )
```

```python
import jax
import jax.numpy as jnp
from jax import lax
from jax.sharding import PartitionSpec as P

BS = 128
HI = lax.Precision.HIGHEST
W_CHUNKS = 1


def per_device(tensor, greens, pattern, block_sizes, trial_vectors):
    shard_rows = tensor.shape[0]
    basis_count = tensor.shape[1]
    group_count = lax.axis_size("blk")
    aux_count = lax.axis_size("aux")
    block_count = block_sizes.shape[0]
    live_mask = (jnp.arange(BS)[None, :] < block_sizes[:, None]).reshape(basis_count)
    row_live = lax.dynamic_slice_in_dim(live_mask, lax.axis_index("blk") * shard_rows, shard_rows)
    col_keep = jnp.broadcast_to(pattern[0, :, 0][:, None] > 0, (block_count, BS)).reshape(basis_count)
    keep = row_live[:, None] & (col_keep & live_mask)[None, :]

    chunk_rows = shard_rows // W_CHUNKS
    pieces = []
    for c in range(W_CHUNKS):
        rows = slice(c * chunk_rows, (c + 1) * chunk_rows)
        part = jnp.einsum(
            "rsp,pk->krs", tensor[rows], trial_vectors, preferred_element_type=jnp.float32
        )
        part = jnp.where(keep[None, rows], part, 0.0)
        part = lax.all_to_all(
            part.astype(jnp.bfloat16), "aux", split_axis=0, concat_axis=0, tiled=True
        )
        pieces.append(jnp.sum(part.astype(jnp.float32), axis=0))
    weighted = jnp.concatenate(pieces, axis=0)
    shifted = [greens] + [
        lax.ppermute(greens, "blk", [(i, (i - s) % group_count) for i in range(group_count)])
        for s in range(1, group_count)
    ]
    both = jnp.roll(jnp.stack(shifted), lax.axis_index("blk"), axis=0)
    both = jnp.concatenate(list(both), axis=2).astype(jnp.float32)
    occupied = both[0]
    virtual = both[1]
    projected = jnp.dot(weighted, virtual, precision=HI)
    projected = projected.reshape(shard_rows, group_count, shard_rows).transpose(1, 0, 2)
    projected = _blk_exchange(projected, group_count)
    projected = projected.reshape(group_count * shard_rows, shard_rows)
    z_rows = jnp.einsum("ln,sl->ns", projected, occupied, precision=HI)
    z_copies = jnp.broadcast_to(z_rows.astype(jnp.bfloat16)[None], (aux_count,) + z_rows.shape)
    z_all = lax.all_to_all(z_copies, "aux", split_axis=0, concat_axis=0, tiled=True)
    z_all = jnp.where(keep[None], z_all, jnp.zeros_like(z_all))
    terms = jnp.einsum(
        "nsp,kns->kp", tensor, z_all, preferred_element_type=jnp.float32
    )
    terms = terms.reshape((group_count, -1) + terms.shape[1:])
    return jnp.sum(_blk_exchange(terms, group_count), axis=0)


def _blk_exchange(blocks, group_count):
    me = lax.axis_index("blk")
    got = [jnp.take(blocks, me, axis=0)]
    for s in range(1, group_count):
        sent = jnp.take(blocks, (me + s) % group_count, axis=0)
        got.append(
            lax.ppermute(sent, "blk", [(i, (i + s) % group_count) for i in range(group_count)])
        )
    ahead = jnp.stack([got[0]] + got[:0:-1])
    return jnp.roll(ahead, me, axis=0)


def solution(mesh):
    placed = (
        P("blk", None, "aux"),
        P(None, None, "blk"),
        P("blk", None, "aux"),
        P(),
        P("aux", None),
    )
    return jax.shard_map(
        per_device, mesh=mesh, in_specs=placed, out_specs=P("blk", "aux"), check_vma=False
    )
```

```python
import jax
import jax.numpy as jnp
from jax import lax
from jax.sharding import PartitionSpec as P

BS = 128
HI = lax.Precision.HIGHEST
W_FIRST_SPLIT = 4


def per_device(tensor, greens, pattern, block_sizes, trial_vectors):
    shard_rows = tensor.shape[0]
    basis_count = tensor.shape[1]
    group_count = lax.axis_size("blk")
    aux_count = lax.axis_size("aux")
    block_count = block_sizes.shape[0]
    live_mask = (jnp.arange(BS)[None, :] < block_sizes[:, None]).reshape(basis_count)
    row_live = lax.dynamic_slice_in_dim(live_mask, lax.axis_index("blk") * shard_rows, shard_rows)
    col_keep = jnp.broadcast_to(pattern[0, :, 0][:, None] > 0, (block_count, BS)).reshape(basis_count)
    keep = row_live[:, None] & (col_keep & live_mask)[None, :]

    first_rows = shard_rows // W_FIRST_SPLIT
    pieces = []
    for rows in (slice(0, first_rows), slice(first_rows, shard_rows)):
        part = jnp.einsum(
            "rsp,pk->krs", tensor[rows], trial_vectors, preferred_element_type=jnp.float32
        )
        part = jnp.where(keep[None, rows], part, 0.0)
        part = lax.all_to_all(
            part.astype(jnp.bfloat16), "aux", split_axis=0, concat_axis=0, tiled=True
        )
        pieces.append(jnp.sum(part.astype(jnp.float32), axis=0))
    weighted = jnp.concatenate(pieces, axis=0)
    shifted = [greens] + [
        lax.ppermute(greens, "blk", [(i, (i - s) % group_count) for i in range(group_count)])
        for s in range(1, group_count)
    ]
    both = jnp.roll(jnp.stack(shifted), lax.axis_index("blk"), axis=0)
    both = jnp.concatenate(list(both), axis=2).astype(jnp.float32)
    occupied = both[0]
    virtual = both[1]
    projected = jnp.dot(weighted, virtual, precision=HI)
    projected = projected.reshape(shard_rows, group_count, shard_rows).transpose(1, 0, 2)
    projected = _blk_exchange(projected, group_count)
    projected = projected.reshape(group_count * shard_rows, shard_rows)
    z_rows = jnp.einsum("ln,sl->ns", projected, occupied, precision=HI)
    z_copies = jnp.broadcast_to(z_rows.astype(jnp.bfloat16)[None], (aux_count,) + z_rows.shape)
    z_all = lax.all_to_all(z_copies, "aux", split_axis=0, concat_axis=0, tiled=True)
    z_all = jnp.where(keep[None], z_all, jnp.zeros_like(z_all))
    terms = jnp.einsum(
        "nsp,kns->kp", tensor, z_all, preferred_element_type=jnp.float32
    )
    terms = terms.reshape((group_count, -1) + terms.shape[1:])
    return jnp.sum(_blk_exchange(terms, group_count), axis=0)


def _blk_exchange(blocks, group_count):
    me = lax.axis_index("blk")
    got = [jnp.take(blocks, me, axis=0)]
    for s in range(1, group_count):
        sent = jnp.take(blocks, (me + s) % group_count, axis=0)
        got.append(
            lax.ppermute(sent, "blk", [(i, (i + s) % group_count) for i in range(group_count)])
        )
    ahead = jnp.stack([got[0]] + got[:0:-1])
    return jnp.roll(ahead, me, axis=0)


def solution(mesh):
    placed = (
        P("blk", None, "aux"),
        P(None, None, "blk"),
        P("blk", None, "aux"),
        P(),
        P("aux", None),
    )
    return jax.shard_map(
        per_device, mesh=mesh, in_specs=placed, out_specs=P("blk", "aux"), check_vma=False
    )
```

```python
import jax
import jax.numpy as jnp
from jax import lax
from jax.sharding import PartitionSpec as P

BS = 128
HI = lax.Precision.HIGHEST
W_CHUNKS = 2


def per_device(tensor, greens, pattern, block_sizes, trial_vectors):
    shard_rows = tensor.shape[0]
    basis_count = tensor.shape[1]
    group_count = lax.axis_size("blk")
    aux_count = lax.axis_size("aux")
    block_count = block_sizes.shape[0]
    live_mask = (jnp.arange(BS)[None, :] < block_sizes[:, None]).reshape(basis_count)
    row_live = lax.dynamic_slice_in_dim(live_mask, lax.axis_index("blk") * shard_rows, shard_rows)
    col_keep = jnp.broadcast_to(pattern[0, :, 0][:, None] > 0, (block_count, BS)).reshape(basis_count)
    keep = row_live[:, None] & (col_keep & live_mask)[None, :]

    chunk_rows = shard_rows // W_CHUNKS
    pieces = []
    for c in range(W_CHUNKS):
        rows = slice(c * chunk_rows, (c + 1) * chunk_rows)
        part = jnp.einsum(
            "rsp,pk->krs", tensor[rows], trial_vectors, preferred_element_type=jnp.float32
        )
        part = jnp.where(keep[None, rows], part, 0.0)
        part = lax.all_to_all(
            part.astype(jnp.bfloat16), "aux", split_axis=0, concat_axis=0, tiled=True
        )
        pieces.append(jnp.sum(part.astype(jnp.float32), axis=0))
    weighted = jnp.concatenate(pieces, axis=0)
    shifted = [greens] + [
        lax.ppermute(greens, "blk", [(i, (i - s) % group_count) for i in range(group_count)])
        for s in range(1, group_count)
    ]
    both = jnp.roll(jnp.stack(shifted), lax.axis_index("blk"), axis=0)
    both = jnp.concatenate(list(both), axis=2).astype(jnp.float32)
    occupied = both[0]
    virtual = both[1]
    projected = jnp.dot(weighted, virtual, precision=HI)
    projected = projected.reshape(shard_rows, group_count, shard_rows).transpose(1, 0, 2)
    projected = _blk_exchange(projected, group_count)
    projected = projected.reshape(group_count * shard_rows, shard_rows)
    z_rows = jnp.einsum("ln,sl->ns", projected, occupied, precision=HI)
    z_copies = jnp.broadcast_to(z_rows.astype(jnp.bfloat16)[None], (aux_count,) + z_rows.shape)
    z_all = lax.all_to_all(z_copies, "aux", split_axis=0, concat_axis=0, tiled=True)
    z_all = jnp.where(keep[None], z_all, jnp.zeros_like(z_all))
    half = shard_rows // 2
    total = None
    for rows in (slice(0, half), slice(half, shard_rows)):
        terms = jnp.einsum(
            "nsp,kns->kp", tensor[rows], z_all[:, rows], preferred_element_type=jnp.float32
        )
        terms = terms.reshape((group_count, -1) + terms.shape[1:])
        part = jnp.sum(_blk_exchange(terms, group_count), axis=0)
        total = part if total is None else total + part
    return total


def _blk_exchange(blocks, group_count):
    me = lax.axis_index("blk")
    got = [jnp.take(blocks, me, axis=0)]
    for s in range(1, group_count):
        sent = jnp.take(blocks, (me + s) % group_count, axis=0)
        got.append(
            lax.ppermute(sent, "blk", [(i, (i + s) % group_count) for i in range(group_count)])
        )
    ahead = jnp.stack([got[0]] + got[:0:-1])
    return jnp.roll(ahead, me, axis=0)


def solution(mesh):
    placed = (
        P("blk", None, "aux"),
        P(None, None, "blk"),
        P("blk", None, "aux"),
        P(),
        P("aux", None),
    )
    return jax.shard_map(
        per_device, mesh=mesh, in_specs=placed, out_specs=P("blk", "aux"), check_vma=False
    )
```

```python
import jax
import jax.numpy as jnp
from jax import lax
from jax.sharding import PartitionSpec as P

BS = 128
HI = lax.Precision.HIGHEST
W_CHUNKS = 2


def per_device(tensor, greens, pattern, block_sizes, trial_vectors):
    shard_rows = tensor.shape[0]
    basis_count = tensor.shape[1]
    group_count = lax.axis_size("blk")
    aux_count = lax.axis_size("aux")
    block_count = block_sizes.shape[0]
    live_mask = (jnp.arange(BS)[None, :] < block_sizes[:, None]).reshape(basis_count)
    row_live = lax.dynamic_slice_in_dim(live_mask, lax.axis_index("blk") * shard_rows, shard_rows)
    col_keep = jnp.broadcast_to(pattern[0, :, 0][:, None] > 0, (block_count, BS)).reshape(basis_count)
    keep = row_live[:, None] & (col_keep & live_mask)[None, :]

    chunk_rows = shard_rows // W_CHUNKS
    pieces = []
    for c in range(W_CHUNKS):
        rows = slice(c * chunk_rows, (c + 1) * chunk_rows)
        part = jnp.einsum(
            "rsp,pk->krs", tensor[rows], trial_vectors, preferred_element_type=jnp.float32
        )
        part = jnp.where(keep[None, rows], part, 0.0)
        part = lax.all_to_all(
            part.astype(jnp.bfloat16), "aux", split_axis=0, concat_axis=0, tiled=True
        )
        pieces.append(jnp.sum(part.astype(jnp.float32), axis=0))
    weighted = jnp.concatenate(pieces, axis=0)
    shifted = [greens] + [
        lax.ppermute(greens, "blk", [(i, (i - s) % group_count) for i in range(group_count)])
        for s in range(1, group_count)
    ]
    both = jnp.concatenate(shifted, axis=2).astype(jnp.float32)
    virtual = both[1]
    projected = jnp.dot(weighted, virtual, precision=HI)
    projected = projected.reshape(shard_rows, group_count, shard_rows).transpose(1, 0, 2)
    got = [projected[0]]
    for s in range(1, group_count):
        got.append(
            lax.ppermute(projected[s], "blk", [(i, (i + s) % group_count) for i in range(group_count)])
        )
    occupied = jnp.concatenate([shifted[(-s) % group_count][0] for s in range(group_count)], axis=1)
    projected = jnp.concatenate(got, axis=0)
    z_rows = jnp.einsum("ln,sl->ns", projected, occupied.astype(jnp.float32), precision=HI)
    z_copies = jnp.broadcast_to(z_rows.astype(jnp.bfloat16)[None], (aux_count,) + z_rows.shape)
    z_all = lax.all_to_all(z_copies, "aux", split_axis=0, concat_axis=0, tiled=True)
    z_all = jnp.where(keep[None], z_all, jnp.zeros_like(z_all))
    terms = jnp.einsum(
        "nsp,kns->kp", tensor, z_all, preferred_element_type=jnp.float32
    )
    terms = terms.reshape((group_count, -1) + terms.shape[1:])
    return jnp.sum(_blk_exchange(terms, group_count), axis=0)


def _blk_exchange(blocks, group_count):
    me = lax.axis_index("blk")
    got = [jnp.take(blocks, me, axis=0)]
    for s in range(1, group_count):
        sent = jnp.take(blocks, (me + s) % group_count, axis=0)
        got.append(
            lax.ppermute(sent, "blk", [(i, (i + s) % group_count) for i in range(group_count)])
        )
    ahead = jnp.stack([got[0]] + got[:0:-1])
    return jnp.roll(ahead, me, axis=0)


def solution(mesh):
    placed = (
        P("blk", None, "aux"),
        P(None, None, "blk"),
        P("blk", None, "aux"),
        P(),
        P("aux", None),
    )
    return jax.shard_map(
        per_device, mesh=mesh, in_specs=placed, out_specs=P("blk", "aux"), check_vma=False
    )
```

```python
import jax
import jax.numpy as jnp
from jax import lax
from jax.sharding import PartitionSpec as P

BS = 128
HI = lax.Precision.HIGHEST
W_CHUNKS = 2


def per_device(tensor, greens, pattern, block_sizes, trial_vectors):
    shard_rows = tensor.shape[0]
    basis_count = tensor.shape[1]
    group_count = lax.axis_size("blk")
    aux_count = lax.axis_size("aux")
    block_count = block_sizes.shape[0]
    live_mask = (jnp.arange(BS)[None, :] < block_sizes[:, None]).reshape(basis_count)
    row_live = lax.dynamic_slice_in_dim(live_mask, lax.axis_index("blk") * shard_rows, shard_rows)
    col_keep = jnp.broadcast_to(pattern[0, :, 0][:, None] > 0, (block_count, BS)).reshape(basis_count)
    keep = row_live[:, None] & (col_keep & live_mask)[None, :]

    chunk_rows = shard_rows // W_CHUNKS
    pieces = []
    for c in range(W_CHUNKS):
        rows = slice(c * chunk_rows, (c + 1) * chunk_rows)
        part = jnp.einsum(
            "rsp,pk->krs", tensor[rows], trial_vectors, preferred_element_type=jnp.float32
        )
        part = jnp.where(keep[None, rows], part, 0.0)
        part = lax.all_to_all(
            part.astype(jnp.bfloat16), "aux", split_axis=0, concat_axis=0, tiled=True
        )
        pieces.append(jnp.sum(part.astype(jnp.float32), axis=0))
    weighted = jnp.concatenate(pieces, axis=0)
    shifted = [greens] + [
        lax.ppermute(greens, "blk", [(i, (i - s) % group_count) for i in range(group_count)])
        for s in range(1, group_count)
    ]
    both = jnp.roll(jnp.stack(shifted), lax.axis_index("blk"), axis=0)
    both = jnp.concatenate(list(both), axis=2).astype(jnp.float32)
    occupied = both[0]
    virtual = both[1]
    projected = jnp.dot(weighted, virtual, precision=HI)
    projected = projected.reshape(shard_rows, group_count, shard_rows).transpose(1, 0, 2)
    projected = _blk_exchange(projected, group_count)
    projected = projected.reshape(group_count * shard_rows, shard_rows)
    z_rows = jnp.einsum("ln,sl->ns", projected, occupied, precision=HI)
    z_copies = jnp.broadcast_to(z_rows.astype(jnp.bfloat16)[None], (aux_count,) + z_rows.shape)
    z_all = lax.all_to_all(z_copies, "aux", split_axis=0, concat_axis=0, tiled=True)
    z_all = jnp.where(keep[None], z_all, jnp.zeros_like(z_all))
    terms = jnp.einsum(
        "nsp,kns->kp", tensor, z_all, preferred_element_type=jnp.float32
    )
    terms = terms.reshape((group_count, -1) + terms.shape[1:])
    me = lax.axis_index("blk")
    total = jnp.take(terms, me, axis=0)
    for s in range(1, group_count):
        sent = jnp.take(terms, (me + s) % group_count, axis=0)
        total = total + lax.ppermute(
            sent, "blk", [(i, (i + s) % group_count) for i in range(group_count)]
        )
    return total


def _blk_exchange(blocks, group_count):
    me = lax.axis_index("blk")
    got = [jnp.take(blocks, me, axis=0)]
    for s in range(1, group_count):
        sent = jnp.take(blocks, (me + s) % group_count, axis=0)
        got.append(
            lax.ppermute(sent, "blk", [(i, (i + s) % group_count) for i in range(group_count)])
        )
    ahead = jnp.stack([got[0]] + got[:0:-1])
    return jnp.roll(ahead, me, axis=0)


def solution(mesh):
    placed = (
        P("blk", None, "aux"),
        P(None, None, "blk"),
        P("blk", None, "aux"),
        P(),
        P("aux", None),
    )
    return jax.shard_map(
        per_device, mesh=mesh, in_specs=placed, out_specs=P("blk", "aux"), check_vma=False
    )
```

```python
import jax
import jax.numpy as jnp
from jax import lax
from jax.sharding import PartitionSpec as P

BS = 128
HI = lax.Precision.HIGHEST
W_CHUNKS = 2


def per_device(tensor, greens, pattern, block_sizes, trial_vectors):
    shard_rows = tensor.shape[0]
    basis_count = tensor.shape[1]
    group_count = lax.axis_size("blk")
    aux_count = lax.axis_size("aux")
    block_count = block_sizes.shape[0]
    live_mask = (jnp.arange(BS)[None, :] < block_sizes[:, None]).reshape(basis_count)
    row_live = lax.dynamic_slice_in_dim(live_mask, lax.axis_index("blk") * shard_rows, shard_rows)
    col_keep = jnp.broadcast_to(pattern[0, :, 0][:, None] > 0, (block_count, BS)).reshape(basis_count)
    keep = row_live[:, None] & (col_keep & live_mask)[None, :]

    chunk_rows = shard_rows // W_CHUNKS
    pieces = []
    for c in range(W_CHUNKS):
        rows = slice(c * chunk_rows, (c + 1) * chunk_rows)
        part = jnp.einsum(
            "rsp,pk->krs", tensor[rows], trial_vectors, preferred_element_type=jnp.float32
        )
        part = jnp.where(keep[None, rows], part, 0.0)
        part = lax.all_to_all(
            part.astype(jnp.bfloat16), "aux", split_axis=0, concat_axis=0, tiled=True
        )
        pieces.append(jnp.sum(part.astype(jnp.float32), axis=0))
    shifted = [greens] + [
        lax.ppermute(greens, "blk", [(i, (i - s) % group_count) for i in range(group_count)])
        for s in range(1, group_count)
    ]
    both = jnp.roll(jnp.stack(shifted), lax.axis_index("blk"), axis=0)
    both = jnp.concatenate(list(both), axis=2).astype(jnp.float32)
    occupied = both[0]
    virtual = both[1]
    moved = []
    for piece in pieces:
        part = jnp.dot(piece, virtual, precision=HI)
        part = part.reshape(piece.shape[0], group_count, shard_rows).transpose(1, 0, 2)
        moved.append(_blk_exchange(part, group_count))
    projected = jnp.concatenate(moved, axis=1).reshape(group_count * shard_rows, shard_rows)
    z_rows = jnp.einsum("ln,sl->ns", projected, occupied, precision=HI)
    z_copies = jnp.broadcast_to(z_rows.astype(jnp.bfloat16)[None], (aux_count,) + z_rows.shape)
    z_all = lax.all_to_all(z_copies, "aux", split_axis=0, concat_axis=0, tiled=True)
    z_all = jnp.where(keep[None], z_all, jnp.zeros_like(z_all))
    terms = jnp.einsum(
        "nsp,kns->kp", tensor, z_all, preferred_element_type=jnp.float32
    )
    terms = terms.reshape((group_count, -1) + terms.shape[1:])
    return jnp.sum(_blk_exchange(terms, group_count), axis=0)


def _blk_exchange(blocks, group_count):
    me = lax.axis_index("blk")
    got = [jnp.take(blocks, me, axis=0)]
    for s in range(1, group_count):
        sent = jnp.take(blocks, (me + s) % group_count, axis=0)
        got.append(
            lax.ppermute(sent, "blk", [(i, (i + s) % group_count) for i in range(group_count)])
        )
    ahead = jnp.stack([got[0]] + got[:0:-1])
    return jnp.roll(ahead, me, axis=0)


def solution(mesh):
    placed = (
        P("blk", None, "aux"),
        P(None, None, "blk"),
        P("blk", None, "aux"),
        P(),
        P("aux", None),
    )
    return jax.shard_map(
        per_device, mesh=mesh, in_specs=placed, out_specs=P("blk", "aux"), check_vma=False
    )
```
